32 devices in a mesh: freq: 2 (over x), row: 4 (over z), col: 4 (over y, core).
Axes of the slice: x: 2, y: 2, z: 4, core: 2. Of those that a mesh axis runs over, the one named last changes fastest.
Arguments:
- sky_maps: bfloat16 [512, 128, 512], P('freq', 'row', 'col'), may hold values from -32 to 32
- beam_sigma: float32 [512], P('freq'), may hold values from 1.5 to 4
- whitening: bfloat16 [512, 512], replicated, may hold values from -0.25 to 0.25
- unmix_init: float32 [128, 512], replicated, may hold values from -0.25 to 0.25
Outputs:
- unmixing: float32 [128, 512], replicated
- sources: bfloat16 [128, 65536], P(None, ('freq', 'row', 'col'))
The draws below stay inside these ranges and needn't reach their ends.
All inputs are finite; a program needn't handle non-finite values.
Results may differ from the reference program's by a relative error of at most 0.0025.
The reference program's roundings to bfloat16 on the way (of `beam_taps`, `rowwise`, `smoothed`, `spectra`, `whitened` and `cubed`) count: a program that leaves them out, or rounds other values in their place, can miss the bound.
Values may be sent and summed in bfloat16 or wider, within the bound.
No kernel may reach another device: no remote copies, remote signals or barrier semaphores. Data moves between devices by JAX's collectives and lax.ppermute only.
A program may use at most 64 MiB of HBM per device.

```python
import math
import jax
import jax.numpy as jnp
from jax import lax

F = 512
COMP = 128
ROWS_DEV = 32
COLS_DEV = 128
HALF = 8
ITERS = 2
NS_STEPS = 5
NR = 128
NC = 512
NPIX = 65536
PIX_DEV = 2048
N_FREQ = 2
N_ROW = 4
N_COL = 4


def draw_sky_maps(key, part):
    spec_key = jax.random.fold_in(key, 11)
    scale_key = jax.random.fold_in(key, 23)
    rough_key = jax.random.fold_in(key, 37)
    freqs = jnp.arange(F, dtype=jnp.float32) / F
    spectral = 2.0 * (1.0 + freqs) ** (-2.5) * jax.random.uniform(spec_key, (F,), jnp.float32, 0.7, 1.4)
    row_pos = jnp.arange(NR, dtype=jnp.float32) / NR
    col_pos = jnp.arange(NC, dtype=jnp.float32) / NC
    ramp = 0.25 + row_pos[:, None] + col_pos[None, :]
    scales = jnp.exp(jax.random.uniform(scale_key, (F, 1, 1), jnp.float32, math.log(2.0), math.log(6.0)))
    rough = jnp.clip(jax.random.normal(rough_key, (F, NR, NC), jnp.float32), -4.0, 4.0)
    return (spectral[:, None, None] * ramp[None] + scales * rough).astype(jnp.bfloat16)


def level_of(rng, dims, split, smallest, high):
    loudness = 1.0
    for dim, parts in split:
        draws = jax.random.uniform(jax.random.fold_in(jax.random.fold_in(rng, 6), dim), (parts,), jnp.float32, smallest / len(split), high / len(split))
        loudness = loudness * jnp.repeat(jnp.exp(draws), dims[dim] // parts).reshape((-1,) + (1,) * (len(dims) - 1 - dim))
    return loudness


def scatter_about(rng, extent, scale, reach, kind=jnp.bfloat16):
    array = scale * jax.random.normal(rng, extent, jnp.float32)
    return jnp.clip(array, min=-reach, max=reach).astype(kind)


def setup_inputs(seed: int = 0) -> dict:
    key_list = jax.random.split(jax.random.key(seed), 5)
    return {
        "sky_maps": draw_sky_maps(jax.random.fold_in(key_list[4], 71), 0),
        "beam_sigma": jnp.clip(jnp.exp(math.log(4.0) - 0.98082925 * jax.random.uniform(key_list[1], (F,), jnp.float32) ** level_of(key_list[1], (F,), ((0, 2),), -0.2, 0.2)), 1.5, 4.0),
        "whitening": scatter_about(key_list[2], (F, F), F ** -0.5, 0.25),
        "unmix_init": scatter_about(key_list[3], (COMP, F), F ** -0.5, 0.25, jnp.float32),
    }


def make_taps(beam_sigma):
    offsets = jnp.arange(2 * HALF + 1, dtype=jnp.float32) - HALF
    shaped = jnp.exp(-(offsets[None, :] * offsets[None, :]) / (2.0 * beam_sigma[:, None] * beam_sigma[:, None]))
    return (shaped / lax.optimization_barrier(jnp.sum(shaped, axis=1, keepdims=True))).astype(jnp.bfloat16)

def smooth_plane(plane, beam_taps):
    values = beam_taps.astype(jnp.float32)
    height = plane.shape[0]
    breadth = plane.shape[1]
    padded = jnp.pad(plane.astype(jnp.float32), ((HALF, HALF), (0, 0)))
    total = jnp.zeros((height, breadth), jnp.float32)
    for offset in range(2 * HALF + 1):
        total = total + values[offset] * padded[offset:offset + height]
    rowwise = total.astype(jnp.bfloat16)
    padded = jnp.pad(rowwise.astype(jnp.float32), ((0, 0), (HALF, HALF)))
    total = jnp.zeros((height, breadth), jnp.float32)
    for offset in range(2 * HALF + 1):
        total = total + values[offset] * padded[:, offset:offset + breadth]
    return total.astype(jnp.bfloat16)

def smooth_bundle(bundle):
    return smooth_plane(bundle[0], bundle[1])

def inverse_root(matrix):
    frob_norm = jnp.sqrt(jnp.sum(matrix * matrix) + 1e-06)
    current = matrix / frob_norm
    unit_matrix = jnp.eye(matrix.shape[0], dtype=jnp.float32)
    inverse = unit_matrix
    for iteration in range(NS_STEPS):
        correction = 0.5 * (3.0 * unit_matrix - jnp.dot(inverse, current, precision=lax.Precision.HIGHEST))
        current = jnp.dot(current, correction, precision=lax.Precision.HIGHEST)
        inverse = jnp.dot(correction, inverse, precision=lax.Precision.HIGHEST)
    return inverse / jnp.sqrt(frob_norm)

def reference(sky_maps, beam_sigma, whitening, unmix_init):
    beam_taps = make_taps(beam_sigma)
    smoothed = lax.map(smooth_bundle, (sky_maps, beam_taps))
    blocks = smoothed.reshape(F, N_ROW, ROWS_DEV, N_COL, COLS_DEV).transpose(0, 1, 3, 2, 4)
    blocks = blocks.reshape(F, N_ROW, N_COL, N_FREQ, PIX_DEV).transpose(0, 3, 1, 2, 4)
    spectra = blocks.reshape(F, NPIX)
    means = lax.optimization_barrier(jnp.sum(spectra, axis=1, dtype=jnp.float32)) / NPIX
    shift = jnp.dot(whitening.astype(jnp.float32), means, precision=lax.Precision.HIGHEST)
    whitened = (jnp.dot(whitening, spectra, preferred_element_type=jnp.float32) - shift[:, None]).astype(jnp.bfloat16)
    unmixing = unmix_init
    for iteration in range(ITERS):
        outputs = jnp.dot(unmixing.astype(jnp.bfloat16), whitened, preferred_element_type=jnp.float32)
        cubed = (outputs * outputs * outputs).astype(jnp.bfloat16)
        moments = lax.dot_general(cubed, whitened, (((1,), (1,)), ((), ())), preferred_element_type=jnp.float32)
        updated = moments / NPIX - 3.0 * unmixing
        gram = jnp.dot(updated, updated.T, precision=lax.Precision.HIGHEST)
        unmixing = jnp.dot(inverse_root(gram), updated, precision=lax.Precision.HIGHEST)
    sources = jnp.dot(unmixing.astype(jnp.bfloat16), whitened, preferred_element_type=jnp.float32).astype(jnp.bfloat16)
    return (unmixing, sources)
```

```python
import jax
import jax.numpy as jnp
from jax import lax
from jax.sharding import PartitionSpec as P

HALF = 8
ITERS = 2
NS_STEPS = 5


def with_halo(cells, sides, width):
    for axis, dim in sides:
        count = lax.axis_size(axis)
        ends = count - 1
        head = lax.slice_in_dim(cells, 0, width, axis=dim)
        tail = lax.slice_in_dim(cells, cells.shape[dim] - width, cells.shape[dim], axis=dim)
        cells = jnp.concatenate(
            [
                lax.ppermute(tail, axis, [(i, (i + 1) % count) for i in range(ends)]),
                cells,
                lax.ppermute(head, axis, [((i + 1) % count, i) for i in range(ends)]),
            ],
            axis=dim,
        )
    return cells


def make_taps(beam_sigma):
    offsets = jnp.arange(2 * HALF + 1, dtype=jnp.float32) - HALF
    shaped = jnp.exp(
        -(offsets[None, :] * offsets[None, :]) / (2.0 * beam_sigma[:, None] * beam_sigma[:, None])
    )
    return (shaped / jnp.sum(shaped, axis=1, keepdims=True)).astype(jnp.bfloat16)


def make_band(beam_taps, length):
    spread = beam_taps.shape[1]
    offsets = jnp.arange(length + spread - 1)[None, :] - jnp.arange(length)[:, None]
    onehot = (offsets[:, :, None] == jnp.arange(spread)[None, None, :]).astype(jnp.float32)
    return jnp.einsum("ijk,ck->cij", onehot, beam_taps.astype(jnp.float32)).astype(jnp.bfloat16)


def inverse_root(matrix):
    frob_norm = jnp.sqrt(jnp.sum(matrix * matrix) + 1e-06)
    current = matrix / frob_norm
    unit_matrix = jnp.eye(matrix.shape[0], dtype=jnp.float32)
    inverse = unit_matrix
    for iteration in range(NS_STEPS):
        correction = 0.5 * (
            3.0 * unit_matrix - jnp.dot(inverse, current, precision=lax.Precision.HIGHEST)
        )
        current = jnp.dot(current, correction, precision=lax.Precision.HIGHEST)
        inverse = jnp.dot(correction, inverse, precision=lax.Precision.HIGHEST)
    return inverse / jnp.sqrt(frob_norm)


def pixel_moments(coarse, whitened):
    outputs = jnp.dot(coarse, whitened, preferred_element_type=jnp.float32)
    cubed = (outputs * outputs * outputs).astype(jnp.bfloat16)
    return lax.dot_general(
        cubed, whitened, (((1,), (1,)), ((), ())), preferred_element_type=jnp.float32
    )


def total_sum(partial, axes):
    count = 1
    for axis in axes:
        count *= lax.axis_size(axis)
    flat = partial.reshape(count, partial.size // count)
    pieces = lax.all_to_all(flat, axes, 0, 0, tiled=True)
    piece = jnp.sum(pieces, axis=0)
    spread = jnp.broadcast_to(piece[None], (count,) + piece.shape)
    gathered = lax.all_to_all(spread, axes, 0, 0, tiled=True)
    return gathered.reshape(partial.shape)


def gathered_sum(partial, axes):
    count = 1
    for axis in axes:
        count *= lax.axis_size(axis)
    spread = jnp.broadcast_to(partial[None], (count,) + partial.shape)
    gathered = lax.all_to_all(spread, axes, 0, 0, tiled=True)
    return jnp.sum(gathered, axis=0)


def shards(sky_maps, beam_sigma, whitening, unmix_init):
    beam_taps = make_taps(beam_sigma)
    channels, height, breadth = sky_maps.shape
    band_rows = make_band(beam_taps, height)
    band_cols = make_band(beam_taps, breadth)
    padded = with_halo(sky_maps, (("row", 1),), HALF)
    rowwise = jnp.einsum(
        "cik,ckj->cij", band_rows, padded, preferred_element_type=jnp.float32
    ).astype(jnp.bfloat16)
    widened = with_halo(rowwise, (("col", 2),), HALF)
    smoothed = jnp.einsum(
        "cim,cjm->cij", widened, band_cols, preferred_element_type=jnp.float32
    ).astype(jnp.bfloat16)
    flattened = smoothed.reshape(channels, height * breadth)
    spectra = lax.all_to_all(flattened, "freq", split_axis=1, concat_axis=0, tiled=True)
    devices = lax.axis_size("freq") * lax.axis_size("row") * lax.axis_size("col")
    total_pixels = spectra.shape[1] * devices
    channel_sums = gathered_sum(jnp.sum(spectra, axis=1, dtype=jnp.float32), ("freq", "row", "col"))
    means = channel_sums / total_pixels
    shift = jnp.dot(whitening.astype(jnp.float32), means, precision=lax.Precision.HIGHEST)
    whitened = (
        jnp.dot(whitening, spectra, preferred_element_type=jnp.float32) - shift[:, None]
    ).astype(jnp.bfloat16)
    unmixing = unmix_init
    for iteration in range(ITERS):
        moments = pixel_moments(unmixing.astype(jnp.bfloat16), whitened)
        moments = total_sum(moments, ("freq", "row", "col"))
        updated = moments / total_pixels - 3.0 * unmixing
        gram = jnp.dot(updated, updated.T, precision=lax.Precision.HIGHEST)
        unmixing = jnp.dot(inverse_root(gram), updated, precision=lax.Precision.HIGHEST)
    sources = jnp.dot(
        unmixing.astype(jnp.bfloat16), whitened, preferred_element_type=jnp.float32
    ).astype(jnp.bfloat16)
    return (unmixing, sources)


def solution(mesh):
    return jax.shard_map(
        shards,
        mesh=mesh,
        in_specs=(P("freq", "row", "col"), P("freq"), P(), P()),
        out_specs=(P(), P(None, ("freq", "row", "col"))),
        check_vma=False,
    )
```

```python
import jax
import jax.numpy as jnp
from jax import lax
from jax.sharding import PartitionSpec as P

HALF = 8
ITERS = 2
NS_STEPS = 5


def with_halo(cells, sides, width):
    for axis, dim in sides:
        count = lax.axis_size(axis)
        ends = count - 1
        head = lax.slice_in_dim(cells, 0, width, axis=dim)
        tail = lax.slice_in_dim(cells, cells.shape[dim] - width, cells.shape[dim], axis=dim)
        cells = jnp.concatenate(
            [
                lax.ppermute(tail, axis, [(i, (i + 1) % count) for i in range(ends)]),
                cells,
                lax.ppermute(head, axis, [((i + 1) % count, i) for i in range(ends)]),
            ],
            axis=dim,
        )
    return cells


def make_taps(beam_sigma):
    offsets = jnp.arange(2 * HALF + 1, dtype=jnp.float32) - HALF
    shaped = jnp.exp(
        -(offsets[None, :] * offsets[None, :]) / (2.0 * beam_sigma[:, None] * beam_sigma[:, None])
    )
    return (shaped / jnp.sum(shaped, axis=1, keepdims=True)).astype(jnp.bfloat16)


def make_band(beam_taps, length):
    spread = beam_taps.shape[1]
    offsets = jnp.arange(length + spread - 1)[None, :] - jnp.arange(length)[:, None]
    onehot = (offsets[:, :, None] == jnp.arange(spread)[None, None, :]).astype(jnp.float32)
    return jnp.einsum("ijk,ck->cij", onehot, beam_taps.astype(jnp.float32)).astype(jnp.bfloat16)


def inverse_root(matrix):
    frob_norm = jnp.sqrt(jnp.sum(matrix * matrix) + 1e-06)
    current = matrix / frob_norm
    unit_matrix = jnp.eye(matrix.shape[0], dtype=jnp.float32)
    inverse = unit_matrix
    for iteration in range(NS_STEPS):
        correction = 0.5 * (
            3.0 * unit_matrix - jnp.dot(inverse, current, precision=lax.Precision.HIGHEST)
        )
        current = jnp.dot(current, correction, precision=lax.Precision.HIGHEST)
        inverse = jnp.dot(correction, inverse, precision=lax.Precision.HIGHEST)
    return inverse / jnp.sqrt(frob_norm)


def pixel_moments(coarse, whitened):
    outputs = jnp.dot(coarse, whitened, preferred_element_type=jnp.float32)
    cubed = (outputs * outputs * outputs).astype(jnp.bfloat16)
    return lax.dot_general(
        cubed, whitened, (((1,), (1,)), ((), ())), preferred_element_type=jnp.float32
    )


def total_sum(partial, axes):
    count = 1
    for axis in axes:
        count *= lax.axis_size(axis)
    flat = partial.reshape(count, partial.size // count)
    pieces = lax.all_to_all(flat, axes, 0, 0, tiled=True)
    piece = jnp.sum(pieces, axis=0)
    spread = jnp.broadcast_to(piece[None], (count,) + piece.shape)
    gathered = lax.all_to_all(spread, axes, 0, 0, tiled=True)
    return gathered.reshape(partial.shape)


def gathered_sum(partial, axes):
    count = 1
    for axis in axes:
        count *= lax.axis_size(axis)
    spread = jnp.broadcast_to(partial[None], (count,) + partial.shape)
    gathered = lax.all_to_all(spread, axes, 0, 0, tiled=True)
    return jnp.sum(gathered, axis=0)


def shards(sky_maps, beam_sigma, whitening, unmix_init):
    beam_taps = make_taps(beam_sigma)
    channels, height, breadth = sky_maps.shape
    band_rows = make_band(beam_taps, height)
    band_cols = make_band(beam_taps, breadth)
    padded = with_halo(sky_maps, (("row", 1),), HALF)
    rowwise = jnp.einsum(
        "cik,ckj->cij", band_rows, padded, preferred_element_type=jnp.float32
    ).astype(jnp.bfloat16)
    widened = with_halo(rowwise, (("col", 2),), HALF)
    smoothed = jnp.einsum(
        "cim,cjm->cij", widened, band_cols, preferred_element_type=jnp.float32
    ).astype(jnp.bfloat16)
    flattened = smoothed.reshape(channels, height * breadth)
    parts = lax.axis_size("freq")
    devices = parts * lax.axis_size("row") * lax.axis_size("col")
    block = height * breadth // parts
    total_pixels = block * devices
    if parts == 2:
        side = lax.axis_index("freq")
        outgoing = lax.dynamic_slice_in_dim(flattened, (1 - side) * block, block, axis=1)
        incoming = lax.ppermute(outgoing, "freq", [(0, 1), (1, 0)])
        local = lax.dynamic_slice_in_dim(flattened, side * block, block, axis=1)
        plane_sums = jnp.sum(flattened, axis=1, dtype=jnp.float32)
        placed = jnp.zeros((parts * channels,), jnp.float32)
        placed = lax.dynamic_update_slice_in_dim(placed, plane_sums, side * channels, axis=0)
        channel_sums = gathered_sum(placed, ("freq", "row", "col"))
        means = channel_sums / total_pixels
        shift = jnp.dot(whitening.astype(jnp.float32), means, precision=lax.Precision.HIGHEST)
        mine = lax.dynamic_slice_in_dim(whitening, side * channels, channels, axis=1)
        theirs = lax.dynamic_slice_in_dim(whitening, (1 - side) * channels, channels, axis=1)
        mixed = jnp.dot(mine, local, preferred_element_type=jnp.float32) + jnp.dot(
            theirs, incoming, preferred_element_type=jnp.float32
        )
    else:
        spectra = lax.all_to_all(flattened, "freq", split_axis=1, concat_axis=0, tiled=True)
        channel_sums = gathered_sum(jnp.sum(spectra, axis=1, dtype=jnp.float32), ("freq", "row", "col"))
        means = channel_sums / total_pixels
        shift = jnp.dot(whitening.astype(jnp.float32), means, precision=lax.Precision.HIGHEST)
        mixed = jnp.dot(whitening, spectra, preferred_element_type=jnp.float32)
    whitened = (mixed - shift[:, None]).astype(jnp.bfloat16)
    unmixing = unmix_init
    for iteration in range(ITERS):
        moments = pixel_moments(unmixing.astype(jnp.bfloat16), whitened)
        moments = total_sum(moments, ("freq", "row", "col"))
        updated = moments / total_pixels - 3.0 * unmixing
        gram = jnp.dot(updated, updated.T, precision=lax.Precision.HIGHEST)
        unmixing = jnp.dot(inverse_root(gram), updated, precision=lax.Precision.HIGHEST)
    sources = jnp.dot(
        unmixing.astype(jnp.bfloat16), whitened, preferred_element_type=jnp.float32
    ).astype(jnp.bfloat16)
    return (unmixing, sources)


def solution(mesh):
    return jax.shard_map(
        shards,
        mesh=mesh,
        in_specs=(P("freq", "row", "col"), P("freq"), P(), P()),
        out_specs=(P(), P(None, ("freq", "row", "col"))),
        check_vma=False,
    )
```

```python
import jax
import jax.numpy as jnp
from jax import lax
from jax.sharding import PartitionSpec as P

HALF = 8
ITERS = 2
NS_STEPS = 5
CHUNKS = 2


def with_halo(cells, sides, width):
    for axis, dim in sides:
        count = lax.axis_size(axis)
        ends = count - 1
        head = lax.slice_in_dim(cells, 0, width, axis=dim)
        tail = lax.slice_in_dim(cells, cells.shape[dim] - width, cells.shape[dim], axis=dim)
        cells = jnp.concatenate(
            [
                lax.ppermute(tail, axis, [(i, (i + 1) % count) for i in range(ends)]),
                cells,
                lax.ppermute(head, axis, [((i + 1) % count, i) for i in range(ends)]),
            ],
            axis=dim,
        )
    return cells


def make_taps(beam_sigma):
    offsets = jnp.arange(2 * HALF + 1, dtype=jnp.float32) - HALF
    shaped = jnp.exp(
        -(offsets[None, :] * offsets[None, :]) / (2.0 * beam_sigma[:, None] * beam_sigma[:, None])
    )
    return (shaped / jnp.sum(shaped, axis=1, keepdims=True)).astype(jnp.bfloat16)


def make_band(beam_taps, length):
    spread = beam_taps.shape[1]
    offsets = jnp.arange(length + spread - 1)[None, :] - jnp.arange(length)[:, None]
    onehot = (offsets[:, :, None] == jnp.arange(spread)[None, None, :]).astype(jnp.float32)
    return jnp.einsum("ijk,ck->cij", onehot, beam_taps.astype(jnp.float32)).astype(jnp.bfloat16)


def inverse_root(matrix):
    frob_norm = jnp.sqrt(jnp.sum(matrix * matrix) + 1e-06)
    current = matrix / frob_norm
    unit_matrix = jnp.eye(matrix.shape[0], dtype=jnp.float32)
    def refine(step, carry):
        current, inverse = carry
        correction = 0.5 * (
            3.0 * unit_matrix - jnp.dot(inverse, current, precision=lax.Precision.HIGHEST)
        )
        current = jnp.dot(current, correction, precision=lax.Precision.HIGHEST)
        inverse = jnp.dot(correction, inverse, precision=lax.Precision.HIGHEST)
        return current, inverse

    current, inverse = lax.fori_loop(0, NS_STEPS, refine, (current, unit_matrix))
    return inverse / jnp.sqrt(frob_norm)


def pixel_moments(coarse, whitened):
    outputs = jnp.dot(coarse, whitened, preferred_element_type=jnp.float32)
    cubed = (outputs * outputs * outputs).astype(jnp.bfloat16)
    return lax.dot_general(
        cubed, whitened, (((1,), (1,)), ((), ())), preferred_element_type=jnp.float32
    )


def total_sum(partial, axes):
    count = 1
    for axis in axes:
        count *= lax.axis_size(axis)
    flat = partial.reshape(count, partial.size // count)
    pieces = lax.all_to_all(flat, axes, 0, 0, tiled=True)
    piece = jnp.sum(pieces, axis=0)
    spread = jnp.broadcast_to(piece[None], (count,) + piece.shape)
    gathered = lax.all_to_all(spread, axes, 0, 0, tiled=True)
    return gathered.reshape(partial.shape)


def gathered_sum(partial, axes):
    count = 1
    for axis in axes:
        count *= lax.axis_size(axis)
    spread = jnp.broadcast_to(partial[None], (count,) + partial.shape)
    gathered = lax.all_to_all(spread, axes, 0, 0, tiled=True)
    return jnp.sum(gathered, axis=0)


def smooth(sky_maps, beam_taps):
    channels, height, breadth = sky_maps.shape
    band_rows = make_band(beam_taps, height)
    band_cols = make_band(beam_taps, breadth)
    padded = with_halo(sky_maps, (("row", 1),), HALF)
    rowwise = jnp.einsum(
        "cik,ckj->cij", band_rows, padded, preferred_element_type=jnp.float32
    ).astype(jnp.bfloat16)
    widened = with_halo(rowwise, (("col", 2),), HALF)
    smoothed = jnp.einsum(
        "cim,cjm->cij", widened, band_cols, preferred_element_type=jnp.float32
    ).astype(jnp.bfloat16)
    return smoothed.reshape(channels, height * breadth)


def shards(sky_maps, beam_sigma, whitening, unmix_init):
    beam_taps = make_taps(beam_sigma)
    channels, height, breadth = sky_maps.shape
    parts = lax.axis_size("freq")
    devices = parts * lax.axis_size("row") * lax.axis_size("col")
    block = height * breadth // parts
    total_pixels = block * devices
    if parts == 2 and channels % CHUNKS == 0:
        side = lax.axis_index("freq")
        width = channels // CHUNKS
        mixed = None
        sums = []
        for chunk in range(CHUNKS):
            low = chunk * width
            flattened = smooth(sky_maps[low:low + width], beam_taps[low:low + width])
            outgoing = lax.dynamic_slice_in_dim(flattened, (1 - side) * block, block, axis=1)
            incoming = lax.ppermute(outgoing, "freq", [(0, 1), (1, 0)])
            local = lax.dynamic_slice_in_dim(flattened, side * block, block, axis=1)
            sums.append(jnp.sum(flattened, axis=1, dtype=jnp.float32))
            mine = lax.dynamic_slice_in_dim(whitening, side * channels + low, width, axis=1)
            theirs = lax.dynamic_slice_in_dim(whitening, (1 - side) * channels + low, width, axis=1)
            part = jnp.dot(mine, local, preferred_element_type=jnp.float32) + jnp.dot(
                theirs, incoming, preferred_element_type=jnp.float32
            )
            mixed = part if mixed is None else mixed + part
        plane_sums = jnp.concatenate(sums)
        placed = jnp.zeros((parts * channels,), jnp.float32)
        placed = lax.dynamic_update_slice_in_dim(placed, plane_sums, side * channels, axis=0)
        channel_sums = gathered_sum(placed, ("freq", "row", "col"))
        means = channel_sums / total_pixels
        shift = jnp.dot(whitening.astype(jnp.float32), means, precision=lax.Precision.HIGHEST)
    else:
        flattened = smooth(sky_maps, beam_taps)
        spectra = lax.all_to_all(flattened, "freq", split_axis=1, concat_axis=0, tiled=True)
        channel_sums = gathered_sum(jnp.sum(spectra, axis=1, dtype=jnp.float32), ("freq", "row", "col"))
        means = channel_sums / total_pixels
        shift = jnp.dot(whitening.astype(jnp.float32), means, precision=lax.Precision.HIGHEST)
        mixed = jnp.dot(whitening, spectra, preferred_element_type=jnp.float32)
    whitened = (mixed - shift[:, None]).astype(jnp.bfloat16)
    def fixed_point(step, unmixing):
        moments = pixel_moments(unmixing.astype(jnp.bfloat16), whitened)
        moments = total_sum(moments, ("freq", "row", "col"))
        updated = moments / total_pixels - 3.0 * unmixing
        gram = jnp.dot(updated, updated.T, precision=lax.Precision.HIGHEST)
        return jnp.dot(inverse_root(gram), updated, precision=lax.Precision.HIGHEST)

    unmixing = lax.fori_loop(0, ITERS, fixed_point, unmix_init)
    sources = jnp.dot(
        unmixing.astype(jnp.bfloat16), whitened, preferred_element_type=jnp.float32
    ).astype(jnp.bfloat16)
    return (unmixing, sources)


def solution(mesh):
    return jax.shard_map(
        shards,
        mesh=mesh,
        in_specs=(P("freq", "row", "col"), P("freq"), P(), P()),
        out_specs=(P(), P(None, ("freq", "row", "col"))),
        check_vma=False,
    )
```

```python
import jax
import jax.numpy as jnp
from jax import lax
from jax.sharding import PartitionSpec as P

HALF = 8
ITERS = 2
NS_STEPS = 5


def with_halo(cells, sides, width):
    for axis, dim in sides:
        count = lax.axis_size(axis)
        ends = count - 1
        head = lax.slice_in_dim(cells, 0, width, axis=dim)
        tail = lax.slice_in_dim(cells, cells.shape[dim] - width, cells.shape[dim], axis=dim)
        cells = jnp.concatenate(
            [
                lax.ppermute(tail, axis, [(i, (i + 1) % count) for i in range(ends)]),
                cells,
                lax.ppermute(head, axis, [((i + 1) % count, i) for i in range(ends)]),
            ],
            axis=dim,
        )
    return cells


def corner(cells, rows, cols, step_row, step_col):
    tall = lax.axis_size("row")
    wide = lax.axis_size("col")
    pairs = []
    for a in range(tall):
        for b in range(wide):
            if 0 <= a + step_row < tall and 0 <= b + step_col < wide:
                pairs.append((a * wide + b, (a + step_row) * wide + b + step_col))
    return lax.ppermute(cells[:, rows, cols], ("row", "col"), pairs)


def with_frame(cells, width):
    height, breadth = cells.shape[1], cells.shape[2]
    top, bottom = slice(0, width), slice(height - width, height)
    left, right = slice(0, width), slice(breadth - width, breadth)
    rows = with_halo(cells, (("row", 1),), width)
    sides = with_halo(cells, (("col", 2),), width)
    upper = jnp.concatenate(
        [corner(cells, bottom, right, 1, 1), rows[:, :width], corner(cells, bottom, left, 1, -1)], axis=2
    )
    lower = jnp.concatenate(
        [corner(cells, top, right, -1, 1), rows[:, -width:], corner(cells, top, left, -1, -1)], axis=2
    )
    return jnp.concatenate([upper, sides, lower], axis=1)


def make_taps(beam_sigma):
    offsets = jnp.arange(2 * HALF + 1, dtype=jnp.float32) - HALF
    shaped = jnp.exp(
        -(offsets[None, :] * offsets[None, :]) / (2.0 * beam_sigma[:, None] * beam_sigma[:, None])
    )
    return (shaped / jnp.sum(shaped, axis=1, keepdims=True)).astype(jnp.bfloat16)


def make_band(beam_taps, length):
    spread = beam_taps.shape[1]
    offsets = jnp.arange(length + spread - 1)[None, :] - jnp.arange(length)[:, None]
    onehot = (offsets[:, :, None] == jnp.arange(spread)[None, None, :]).astype(jnp.float32)
    return jnp.einsum("ijk,ck->cij", onehot, beam_taps.astype(jnp.float32)).astype(jnp.bfloat16)


def inverse_root(matrix):
    frob_norm = jnp.sqrt(jnp.sum(matrix * matrix) + 1e-06)
    current = matrix / frob_norm
    unit_matrix = jnp.eye(matrix.shape[0], dtype=jnp.float32)
    inverse = unit_matrix
    for iteration in range(NS_STEPS):
        correction = 0.5 * (
            3.0 * unit_matrix - jnp.dot(inverse, current, precision=lax.Precision.HIGHEST)
        )
        current = jnp.dot(current, correction, precision=lax.Precision.HIGHEST)
        inverse = jnp.dot(correction, inverse, precision=lax.Precision.HIGHEST)
    return inverse / jnp.sqrt(frob_norm)


def pixel_moments(coarse, whitened):
    outputs = jnp.dot(coarse, whitened, preferred_element_type=jnp.float32)
    cubed = (outputs * outputs * outputs).astype(jnp.bfloat16)
    return lax.dot_general(
        cubed, whitened, (((1,), (1,)), ((), ())), preferred_element_type=jnp.float32
    )


def total_sum(partial, axes):
    count = 1
    for axis in axes:
        count *= lax.axis_size(axis)
    flat = partial.reshape(count, partial.size // count)
    pieces = lax.all_to_all(flat, axes, 0, 0, tiled=True)
    piece = jnp.sum(pieces, axis=0)
    spread = jnp.broadcast_to(piece[None], (count,) + piece.shape)
    gathered = lax.all_to_all(spread, axes, 0, 0, tiled=True)
    return gathered.reshape(partial.shape)


def gathered_sum(partial, axes):
    count = 1
    for axis in axes:
        count *= lax.axis_size(axis)
    spread = jnp.broadcast_to(partial[None], (count,) + partial.shape)
    gathered = lax.all_to_all(spread, axes, 0, 0, tiled=True)
    return jnp.sum(gathered, axis=0)


def shards(sky_maps, beam_sigma, whitening, unmix_init):
    beam_taps = make_taps(beam_sigma)
    channels, height, breadth = sky_maps.shape
    band_rows = make_band(beam_taps, height)
    band_cols = make_band(beam_taps, breadth)
    framed = with_frame(sky_maps, HALF)
    widened = jnp.einsum(
        "cik,ckj->cij", band_rows, framed, preferred_element_type=jnp.float32
    ).astype(jnp.bfloat16)
    smoothed = jnp.einsum(
        "cim,cjm->cij", widened, band_cols, preferred_element_type=jnp.float32
    ).astype(jnp.bfloat16)
    flattened = smoothed.reshape(channels, height * breadth)
    parts = lax.axis_size("freq")
    devices = parts * lax.axis_size("row") * lax.axis_size("col")
    block = height * breadth // parts
    total_pixels = block * devices
    if parts == 2:
        side = lax.axis_index("freq")
        outgoing = lax.dynamic_slice_in_dim(flattened, (1 - side) * block, block, axis=1)
        incoming = lax.ppermute(outgoing, "freq", [(0, 1), (1, 0)])
        local = lax.dynamic_slice_in_dim(flattened, side * block, block, axis=1)
        plane_sums = jnp.sum(flattened, axis=1, dtype=jnp.float32)
        placed = jnp.zeros((parts * channels,), jnp.float32)
        placed = lax.dynamic_update_slice_in_dim(placed, plane_sums, side * channels, axis=0)
        channel_sums = gathered_sum(placed, ("freq", "row", "col"))
        means = channel_sums / total_pixels
        shift = jnp.dot(whitening.astype(jnp.float32), means, precision=lax.Precision.HIGHEST)
        mine = lax.dynamic_slice_in_dim(whitening, side * channels, channels, axis=1)
        theirs = lax.dynamic_slice_in_dim(whitening, (1 - side) * channels, channels, axis=1)
        mixed = jnp.dot(mine, local, preferred_element_type=jnp.float32) + jnp.dot(
            theirs, incoming, preferred_element_type=jnp.float32
        )
    else:
        spectra = lax.all_to_all(flattened, "freq", split_axis=1, concat_axis=0, tiled=True)
        channel_sums = gathered_sum(jnp.sum(spectra, axis=1, dtype=jnp.float32), ("freq", "row", "col"))
        means = channel_sums / total_pixels
        shift = jnp.dot(whitening.astype(jnp.float32), means, precision=lax.Precision.HIGHEST)
        mixed = jnp.dot(whitening, spectra, preferred_element_type=jnp.float32)
    whitened = (mixed - shift[:, None]).astype(jnp.bfloat16)
    unmixing = unmix_init
    for iteration in range(ITERS):
        moments = pixel_moments(unmixing.astype(jnp.bfloat16), whitened)
        moments = total_sum(moments, ("freq", "row", "col"))
        updated = moments / total_pixels - 3.0 * unmixing
        gram = jnp.dot(updated, updated.T, precision=lax.Precision.HIGHEST)
        unmixing = jnp.dot(inverse_root(gram), updated, precision=lax.Precision.HIGHEST)
    sources = jnp.dot(
        unmixing.astype(jnp.bfloat16), whitened, preferred_element_type=jnp.float32
    ).astype(jnp.bfloat16)
    return (unmixing, sources)


def solution(mesh):
    return jax.shard_map(
        shards,
        mesh=mesh,
        in_specs=(P("freq", "row", "col"), P("freq"), P(), P()),
        out_specs=(P(), P(None, ("freq", "row", "col"))),
        check_vma=False,
    )
```

```python
import jax
import jax.numpy as jnp
from jax import lax
from jax.sharding import PartitionSpec as P

HALF = 8
ITERS = 2
NS_STEPS = 5


def with_halo(cells, sides, width):
    for axis, dim in sides:
        count = lax.axis_size(axis)
        ends = count - 1
        head = lax.slice_in_dim(cells, 0, width, axis=dim)
        tail = lax.slice_in_dim(cells, cells.shape[dim] - width, cells.shape[dim], axis=dim)
        cells = jnp.concatenate(
            [
                lax.ppermute(tail, axis, [(i, (i + 1) % count) for i in range(ends)]),
                cells,
                lax.ppermute(head, axis, [((i + 1) % count, i) for i in range(ends)]),
            ],
            axis=dim,
        )
    return cells


def make_taps(beam_sigma):
    offsets = jnp.arange(2 * HALF + 1, dtype=jnp.float32) - HALF
    shaped = jnp.exp(
        -(offsets[None, :] * offsets[None, :]) / (2.0 * beam_sigma[:, None] * beam_sigma[:, None])
    )
    return (shaped / jnp.sum(shaped, axis=1, keepdims=True)).astype(jnp.bfloat16)


def make_band(beam_taps, length):
    spread = beam_taps.shape[1]
    offsets = jnp.arange(length + spread - 1)[None, :] - jnp.arange(length)[:, None]
    onehot = (offsets[:, :, None] == jnp.arange(spread)[None, None, :]).astype(jnp.float32)
    return jnp.einsum("ijk,ck->cij", onehot, beam_taps.astype(jnp.float32)).astype(jnp.bfloat16)


def depthwise(cells, kernel):
    out = lax.conv_general_dilated(
        cells[None],
        kernel,
        window_strides=(1, 1),
        padding="VALID",
        dimension_numbers=("NCHW", "OIHW", "NCHW"),
        feature_group_count=cells.shape[0],
        preferred_element_type=jnp.float32,
    )
    return out[0].astype(jnp.bfloat16)


def inverse_root(matrix):
    frob_norm = jnp.sqrt(jnp.sum(matrix * matrix) + 1e-06)
    current = matrix / frob_norm
    unit_matrix = jnp.eye(matrix.shape[0], dtype=jnp.float32)
    inverse = unit_matrix
    for iteration in range(NS_STEPS):
        correction = 0.5 * (
            3.0 * unit_matrix - jnp.dot(inverse, current, precision=lax.Precision.HIGHEST)
        )
        current = jnp.dot(current, correction, precision=lax.Precision.HIGHEST)
        inverse = jnp.dot(correction, inverse, precision=lax.Precision.HIGHEST)
    return inverse / jnp.sqrt(frob_norm)


def pixel_moments(coarse, whitened):
    outputs = jnp.dot(coarse, whitened, preferred_element_type=jnp.float32)
    cubed = (outputs * outputs * outputs).astype(jnp.bfloat16)
    return lax.dot_general(
        cubed, whitened, (((1,), (1,)), ((), ())), preferred_element_type=jnp.float32
    )


def total_sum(partial, axes):
    count = 1
    for axis in axes:
        count *= lax.axis_size(axis)
    flat = partial.reshape(count, partial.size // count)
    pieces = lax.all_to_all(flat, axes, 0, 0, tiled=True)
    piece = jnp.sum(pieces, axis=0)
    spread = jnp.broadcast_to(piece[None], (count,) + piece.shape)
    gathered = lax.all_to_all(spread, axes, 0, 0, tiled=True)
    return gathered.reshape(partial.shape)


def gathered_sum(partial, axes):
    count = 1
    for axis in axes:
        count *= lax.axis_size(axis)
    spread = jnp.broadcast_to(partial[None], (count,) + partial.shape)
    gathered = lax.all_to_all(spread, axes, 0, 0, tiled=True)
    return jnp.sum(gathered, axis=0)


def shards(sky_maps, beam_sigma, whitening, unmix_init):
    beam_taps = lax.optimization_barrier(make_taps(beam_sigma))
    channels, height, breadth = sky_maps.shape
    padded = with_halo(sky_maps, (("row", 1),), HALF)
    rowwise = depthwise(padded, beam_taps[:, None, :, None])
    widened = with_halo(rowwise, (("col", 2),), HALF)
    smoothed = depthwise(widened, beam_taps[:, None, None, :])
    flattened = smoothed.reshape(channels, height * breadth)
    parts = lax.axis_size("freq")
    devices = parts * lax.axis_size("row") * lax.axis_size("col")
    block = height * breadth // parts
    total_pixels = block * devices
    if parts == 2:
        side = lax.axis_index("freq")
        outgoing = lax.dynamic_slice_in_dim(flattened, (1 - side) * block, block, axis=1)
        incoming = lax.ppermute(outgoing, "freq", [(0, 1), (1, 0)])
        local = lax.dynamic_slice_in_dim(flattened, side * block, block, axis=1)
        plane_sums = jnp.sum(lax.optimization_barrier(flattened), axis=1, dtype=jnp.float32)
        placed = jnp.zeros((parts * channels,), jnp.float32)
        placed = lax.dynamic_update_slice_in_dim(placed, plane_sums, side * channels, axis=0)
        channel_sums = gathered_sum(placed, ("freq", "row", "col"))
        means = channel_sums / total_pixels
        shift = jnp.dot(whitening.astype(jnp.float32), means, precision=lax.Precision.HIGHEST)
        mine = lax.dynamic_slice_in_dim(whitening, side * channels, channels, axis=1)
        theirs = lax.dynamic_slice_in_dim(whitening, (1 - side) * channels, channels, axis=1)
        mixed = jnp.dot(mine, local, preferred_element_type=jnp.float32) + jnp.dot(
            theirs, incoming, preferred_element_type=jnp.float32
        )
    else:
        spectra = lax.all_to_all(flattened, "freq", split_axis=1, concat_axis=0, tiled=True)
        channel_sums = gathered_sum(jnp.sum(spectra, axis=1, dtype=jnp.float32), ("freq", "row", "col"))
        means = channel_sums / total_pixels
        shift = jnp.dot(whitening.astype(jnp.float32), means, precision=lax.Precision.HIGHEST)
        mixed = jnp.dot(whitening, spectra, preferred_element_type=jnp.float32)
    whitened = (mixed - shift[:, None]).astype(jnp.bfloat16)
    unmixing = unmix_init
    for iteration in range(ITERS):
        moments = pixel_moments(unmixing.astype(jnp.bfloat16), whitened)
        moments = total_sum(moments, ("freq", "row", "col"))
        updated = moments / total_pixels - 3.0 * unmixing
        gram = jnp.dot(updated, updated.T, precision=lax.Precision.HIGHEST)
        unmixing = jnp.dot(inverse_root(gram), updated, precision=lax.Precision.HIGHEST)
    sources = jnp.dot(
        unmixing.astype(jnp.bfloat16), whitened, preferred_element_type=jnp.float32
    ).astype(jnp.bfloat16)
    return (unmixing, sources)


def solution(mesh):
    return jax.shard_map(
        shards,
        mesh=mesh,
        in_specs=(P("freq", "row", "col"), P("freq"), P(), P()),
        out_specs=(P(), P(None, ("freq", "row", "col"))),
        check_vma=False,
    )
```

```python
import jax
import jax.numpy as jnp
from jax import lax
from jax.sharding import PartitionSpec as P

HALF = 8
ITERS = 2
NS_STEPS = 5


def with_halo(cells, sides, width):
    for axis, dim in sides:
        count = lax.axis_size(axis)
        ends = count - 1
        head = lax.slice_in_dim(cells, 0, width, axis=dim)
        tail = lax.slice_in_dim(cells, cells.shape[dim] - width, cells.shape[dim], axis=dim)
        cells = jnp.concatenate(
            [
                lax.ppermute(tail, axis, [(i, (i + 1) % count) for i in range(ends)]),
                cells,
                lax.ppermute(head, axis, [((i + 1) % count, i) for i in range(ends)]),
            ],
            axis=dim,
        )
    return cells


def make_taps(beam_sigma):
    offsets = jnp.arange(2 * HALF + 1, dtype=jnp.float32) - HALF
    shaped = jnp.exp(
        -(offsets[None, :] * offsets[None, :]) / (2.0 * beam_sigma[:, None] * beam_sigma[:, None])
    )
    return (shaped / jnp.sum(shaped, axis=1, keepdims=True)).astype(jnp.bfloat16)


def make_band(beam_taps, length):
    spread = beam_taps.shape[1]
    offsets = jnp.arange(length + spread - 1)[None, :] - jnp.arange(length)[:, None]
    onehot = (offsets[:, :, None] == jnp.arange(spread)[None, None, :]).astype(jnp.float32)
    return jnp.einsum("ijk,ck->cij", onehot, beam_taps.astype(jnp.float32)).astype(jnp.bfloat16)


def depthwise(cells, kernel):
    out = lax.conv_general_dilated(
        cells[None],
        kernel,
        window_strides=(1, 1),
        padding="VALID",
        dimension_numbers=("NCHW", "OIHW", "NCHW"),
        feature_group_count=cells.shape[0],
        preferred_element_type=jnp.float32,
    )
    return out[0].astype(jnp.bfloat16)


def split_pass(cells, kernel, axis, dim):
    length = cells.shape[dim]
    if length < 4 * HALF:
        return depthwise(with_halo(cells, ((axis, dim),), HALF), kernel)
    count = lax.axis_size(axis)
    ends = count - 1
    head = lax.slice_in_dim(cells, 0, 2 * HALF, axis=dim)
    tail = lax.slice_in_dim(cells, length - 2 * HALF, length, axis=dim)
    before = lax.ppermute(
        lax.slice_in_dim(tail, HALF, 2 * HALF, axis=dim), axis, [(i, (i + 1) % count) for i in range(ends)]
    )
    after = lax.ppermute(
        lax.slice_in_dim(head, 0, HALF, axis=dim), axis, [((i + 1) % count, i) for i in range(ends)]
    )
    middle = depthwise(cells, kernel)
    first = depthwise(jnp.concatenate([before, head], axis=dim), kernel)
    last = depthwise(jnp.concatenate([tail, after], axis=dim), kernel)
    return jnp.concatenate([first, middle, last], axis=dim)


def inverse_root(matrix):
    frob_norm = jnp.sqrt(jnp.sum(matrix * matrix) + 1e-06)
    current = matrix / frob_norm
    unit_matrix = jnp.eye(matrix.shape[0], dtype=jnp.float32)
    inverse = unit_matrix
    for iteration in range(NS_STEPS):
        correction = 0.5 * (
            3.0 * unit_matrix - jnp.dot(inverse, current, precision=lax.Precision.HIGHEST)
        )
        current = jnp.dot(current, correction, precision=lax.Precision.HIGHEST)
        inverse = jnp.dot(correction, inverse, precision=lax.Precision.HIGHEST)
    return inverse / jnp.sqrt(frob_norm)


def pixel_moments(coarse, whitened):
    outputs = jnp.dot(coarse, whitened, preferred_element_type=jnp.float32)
    cubed = (outputs * outputs * outputs).astype(jnp.bfloat16)
    return lax.dot_general(
        cubed, whitened, (((1,), (1,)), ((), ())), preferred_element_type=jnp.float32
    )


def total_sum(partial, axes):
    count = 1
    for axis in axes:
        count *= lax.axis_size(axis)
    flat = partial.reshape(count, partial.size // count)
    pieces = lax.all_to_all(flat, axes, 0, 0, tiled=True)
    piece = jnp.sum(pieces, axis=0)
    spread = jnp.broadcast_to(piece[None], (count,) + piece.shape)
    gathered = lax.all_to_all(spread, axes, 0, 0, tiled=True)
    return gathered.reshape(partial.shape)


def gathered_sum(partial, axes):
    count = 1
    for axis in axes:
        count *= lax.axis_size(axis)
    spread = jnp.broadcast_to(partial[None], (count,) + partial.shape)
    gathered = lax.all_to_all(spread, axes, 0, 0, tiled=True)
    return jnp.sum(gathered, axis=0)


def shards(sky_maps, beam_sigma, whitening, unmix_init):
    beam_taps = lax.optimization_barrier(make_taps(beam_sigma))
    channels, height, breadth = sky_maps.shape
    rowwise = split_pass(sky_maps, beam_taps[:, None, :, None], "row", 1)
    smoothed = split_pass(rowwise, beam_taps[:, None, None, :], "col", 2)
    flattened = smoothed.reshape(channels, height * breadth)
    parts = lax.axis_size("freq")
    devices = parts * lax.axis_size("row") * lax.axis_size("col")
    block = height * breadth // parts
    total_pixels = block * devices
    if parts == 2:
        side = lax.axis_index("freq")
        outgoing = lax.dynamic_slice_in_dim(flattened, (1 - side) * block, block, axis=1)
        incoming = lax.ppermute(outgoing, "freq", [(0, 1), (1, 0)])
        local = lax.dynamic_slice_in_dim(flattened, side * block, block, axis=1)
        plane_sums = jnp.sum(lax.optimization_barrier(flattened), axis=1, dtype=jnp.float32)
        placed = jnp.zeros((parts * channels,), jnp.float32)
        placed = lax.dynamic_update_slice_in_dim(placed, plane_sums, side * channels, axis=0)
        channel_sums = gathered_sum(placed, ("freq", "row", "col"))
        means = channel_sums / total_pixels
        shift = jnp.dot(whitening.astype(jnp.float32), means, precision=lax.Precision.HIGHEST)
        mine = lax.dynamic_slice_in_dim(whitening, side * channels, channels, axis=1)
        theirs = lax.dynamic_slice_in_dim(whitening, (1 - side) * channels, channels, axis=1)
        mixed = jnp.dot(mine, local, preferred_element_type=jnp.float32) + jnp.dot(
            theirs, incoming, preferred_element_type=jnp.float32
        )
    else:
        spectra = lax.all_to_all(flattened, "freq", split_axis=1, concat_axis=0, tiled=True)
        channel_sums = gathered_sum(jnp.sum(spectra, axis=1, dtype=jnp.float32), ("freq", "row", "col"))
        means = channel_sums / total_pixels
        shift = jnp.dot(whitening.astype(jnp.float32), means, precision=lax.Precision.HIGHEST)
        mixed = jnp.dot(whitening, spectra, preferred_element_type=jnp.float32)
    whitened = (mixed - shift[:, None]).astype(jnp.bfloat16)
    unmixing = unmix_init
    for iteration in range(ITERS):
        moments = pixel_moments(unmixing.astype(jnp.bfloat16), whitened)
        moments = total_sum(moments, ("freq", "row", "col"))
        updated = moments / total_pixels - 3.0 * unmixing
        gram = jnp.dot(updated, updated.T, precision=lax.Precision.HIGHEST)
        unmixing = jnp.dot(inverse_root(gram), updated, precision=lax.Precision.HIGHEST)
    sources = jnp.dot(
        unmixing.astype(jnp.bfloat16), whitened, preferred_element_type=jnp.float32
    ).astype(jnp.bfloat16)
    return (unmixing, sources)


def solution(mesh):
    return jax.shard_map(
        shards,
        mesh=mesh,
        in_specs=(P("freq", "row", "col"), P("freq"), P(), P()),
        out_specs=(P(), P(None, ("freq", "row", "col"))),
        check_vma=False,
    )
```

```python
import jax
import jax.numpy as jnp
from jax import lax
from jax.sharding import PartitionSpec as P

HALF = 8
ITERS = 2
NS_STEPS = 5


def with_halo(cells, sides, width):
    for axis, dim in sides:
        count = lax.axis_size(axis)
        ends = count - 1
        head = lax.slice_in_dim(cells, 0, width, axis=dim)
        tail = lax.slice_in_dim(cells, cells.shape[dim] - width, cells.shape[dim], axis=dim)
        cells = jnp.concatenate(
            [
                lax.ppermute(tail, axis, [(i, (i + 1) % count) for i in range(ends)]),
                cells,
                lax.ppermute(head, axis, [((i + 1) % count, i) for i in range(ends)]),
            ],
            axis=dim,
        )
    return cells


def make_taps(beam_sigma):
    offsets = jnp.arange(2 * HALF + 1, dtype=jnp.float32) - HALF
    shaped = jnp.exp(
        -(offsets[None, :] * offsets[None, :]) / (2.0 * beam_sigma[:, None] * beam_sigma[:, None])
    )
    return (shaped / jnp.sum(shaped, axis=1, keepdims=True)).astype(jnp.bfloat16)


def make_band(beam_taps, length):
    spread = beam_taps.shape[1]
    offsets = jnp.arange(length + spread - 1)[None, :] - jnp.arange(length)[:, None]
    onehot = (offsets[:, :, None] == jnp.arange(spread)[None, None, :]).astype(jnp.float32)
    return jnp.einsum("ijk,ck->cij", onehot, beam_taps.astype(jnp.float32)).astype(jnp.bfloat16)


def depthwise(cells, kernel):
    out = lax.conv_general_dilated(
        cells[None],
        kernel,
        window_strides=(1, 1),
        padding="VALID",
        dimension_numbers=("NCHW", "OIHW", "NCHW"),
        feature_group_count=cells.shape[0],
        preferred_element_type=jnp.float32,
    )
    return out[0].astype(jnp.bfloat16)


def halos(cells, axis, dim):
    length = cells.shape[dim]
    count = lax.axis_size(axis)
    ends = count - 1
    before = lax.ppermute(
        lax.slice_in_dim(cells, length - HALF, length, axis=dim), axis, [(i, (i + 1) % count) for i in range(ends)]
    )
    after = lax.ppermute(
        lax.slice_in_dim(cells, 0, HALF, axis=dim), axis, [((i + 1) % count, i) for i in range(ends)]
    )
    return before, after


def assemble(cells, before, after, kernel, dim):
    length = cells.shape[dim]
    if length < 4 * HALF:
        return depthwise(jnp.concatenate([before, cells, after], axis=dim), kernel)
    head = lax.slice_in_dim(cells, 0, 2 * HALF, axis=dim)
    tail = lax.slice_in_dim(cells, length - 2 * HALF, length, axis=dim)
    middle = depthwise(cells, kernel)
    first = depthwise(jnp.concatenate([before, head], axis=dim), kernel)
    last = depthwise(jnp.concatenate([tail, after], axis=dim), kernel)
    return jnp.concatenate([first, middle, last], axis=dim)


def split_pass(cells, kernel, axis, dim):
    before, after = halos(cells, axis, dim)
    return assemble(cells, before, after, kernel, dim)


def band_of_rows(cells, before, after, kernel, start, rows):
    pick = lambda part: lax.dynamic_slice_in_dim(part, start, rows, axis=1)
    return assemble(pick(cells), pick(before), pick(after), kernel, 2)


def inverse_root(matrix):
    frob_norm = jnp.sqrt(jnp.sum(matrix * matrix) + 1e-06)
    current = matrix / frob_norm
    unit_matrix = jnp.eye(matrix.shape[0], dtype=jnp.float32)
    inverse = unit_matrix
    for iteration in range(NS_STEPS):
        correction = 0.5 * (
            3.0 * unit_matrix - jnp.dot(inverse, current, precision=lax.Precision.HIGHEST)
        )
        current = jnp.dot(current, correction, precision=lax.Precision.HIGHEST)
        inverse = jnp.dot(correction, inverse, precision=lax.Precision.HIGHEST)
    return inverse / jnp.sqrt(frob_norm)


def pixel_moments(coarse, whitened):
    outputs = jnp.dot(coarse, whitened, preferred_element_type=jnp.float32)
    cubed = (outputs * outputs * outputs).astype(jnp.bfloat16)
    return lax.dot_general(
        cubed, whitened, (((1,), (1,)), ((), ())), preferred_element_type=jnp.float32
    )


def total_sum(partial, axes):
    count = 1
    for axis in axes:
        count *= lax.axis_size(axis)
    flat = partial.reshape(count, partial.size // count)
    pieces = lax.all_to_all(flat, axes, 0, 0, tiled=True)
    piece = jnp.sum(pieces, axis=0)
    spread = jnp.broadcast_to(piece[None], (count,) + piece.shape)
    gathered = lax.all_to_all(spread, axes, 0, 0, tiled=True)
    return gathered.reshape(partial.shape)


def gathered_sum(partial, axes):
    count = 1
    for axis in axes:
        count *= lax.axis_size(axis)
    spread = jnp.broadcast_to(partial[None], (count,) + partial.shape)
    gathered = lax.all_to_all(spread, axes, 0, 0, tiled=True)
    return jnp.sum(gathered, axis=0)


def shards(sky_maps, beam_sigma, whitening, unmix_init):
    beam_taps = lax.optimization_barrier(make_taps(beam_sigma))
    channels, height, breadth = sky_maps.shape
    rowwise = split_pass(sky_maps, beam_taps[:, None, :, None], "row", 1)
    column_kernel = beam_taps[:, None, None, :]
    parts = lax.axis_size("freq")
    devices = parts * lax.axis_size("row") * lax.axis_size("col")
    block = height * breadth // parts
    total_pixels = block * devices
    if parts == 2 and height % parts == 0:
        side = lax.axis_index("freq")
        half = height // parts
        before, after = halos(rowwise, "col", 2)
        outgoing = band_of_rows(rowwise, before, after, column_kernel, (1 - side) * half, half)
        outgoing = outgoing.reshape(channels, block)
        incoming = lax.ppermute(outgoing, "freq", [(0, 1), (1, 0)])
        local = band_of_rows(rowwise, before, after, column_kernel, side * half, half)
        local = local.reshape(channels, block)
        plane_sums = jnp.sum(outgoing, axis=1, dtype=jnp.float32) + jnp.sum(local, axis=1, dtype=jnp.float32)
        placed = jnp.zeros((parts * channels,), jnp.float32)
        placed = lax.dynamic_update_slice_in_dim(placed, plane_sums, side * channels, axis=0)
        channel_sums = gathered_sum(placed, ("freq", "row", "col"))
        means = channel_sums / total_pixels
        shift = jnp.dot(whitening.astype(jnp.float32), means, precision=lax.Precision.HIGHEST)
        mine = lax.dynamic_slice_in_dim(whitening, side * channels, channels, axis=1)
        theirs = lax.dynamic_slice_in_dim(whitening, (1 - side) * channels, channels, axis=1)
        mixed = jnp.dot(mine, local, preferred_element_type=jnp.float32) + jnp.dot(
            theirs, incoming, preferred_element_type=jnp.float32
        )
    else:
        smoothed = split_pass(rowwise, column_kernel, "col", 2)
        flattened = smoothed.reshape(channels, height * breadth)
        spectra = lax.all_to_all(flattened, "freq", split_axis=1, concat_axis=0, tiled=True)
        channel_sums = gathered_sum(jnp.sum(spectra, axis=1, dtype=jnp.float32), ("freq", "row", "col"))
        means = channel_sums / total_pixels
        shift = jnp.dot(whitening.astype(jnp.float32), means, precision=lax.Precision.HIGHEST)
        mixed = jnp.dot(whitening, spectra, preferred_element_type=jnp.float32)
    whitened = (mixed - shift[:, None]).astype(jnp.bfloat16)
    unmixing = unmix_init
    for iteration in range(ITERS):
        moments = pixel_moments(unmixing.astype(jnp.bfloat16), whitened)
        moments = total_sum(moments, ("freq", "row", "col"))
        updated = moments / total_pixels - 3.0 * unmixing
        gram = jnp.dot(updated, updated.T, precision=lax.Precision.HIGHEST)
        unmixing = jnp.dot(inverse_root(gram), updated, precision=lax.Precision.HIGHEST)
    sources = jnp.dot(
        unmixing.astype(jnp.bfloat16), whitened, preferred_element_type=jnp.float32
    ).astype(jnp.bfloat16)
    return (unmixing, sources)


def solution(mesh):
    return jax.shard_map(
        shards,
        mesh=mesh,
        in_specs=(P("freq", "row", "col"), P("freq"), P(), P()),
        out_specs=(P(), P(None, ("freq", "row", "col"))),
        check_vma=False,
    )
```

```python
import jax
import jax.numpy as jnp
from jax import lax
from jax.sharding import PartitionSpec as P

HALF = 8
ITERS = 2
NS_STEPS = 5


def with_halo(cells, sides, width):
    for axis, dim in sides:
        count = lax.axis_size(axis)
        ends = count - 1
        head = lax.slice_in_dim(cells, 0, width, axis=dim)
        tail = lax.slice_in_dim(cells, cells.shape[dim] - width, cells.shape[dim], axis=dim)
        cells = jnp.concatenate(
            [
                lax.ppermute(tail, axis, [(i, (i + 1) % count) for i in range(ends)]),
                cells,
                lax.ppermute(head, axis, [((i + 1) % count, i) for i in range(ends)]),
            ],
            axis=dim,
        )
    return cells


def make_taps(beam_sigma):
    offsets = jnp.arange(2 * HALF + 1, dtype=jnp.float32) - HALF
    shaped = jnp.exp(
        -(offsets[None, :] * offsets[None, :]) / (2.0 * beam_sigma[:, None] * beam_sigma[:, None])
    )
    return (shaped / jnp.sum(shaped, axis=1, keepdims=True)).astype(jnp.bfloat16)


def make_band(beam_taps, length):
    spread = beam_taps.shape[1]
    offsets = jnp.arange(length + spread - 1)[None, :] - jnp.arange(length)[:, None]
    onehot = (offsets[:, :, None] == jnp.arange(spread)[None, None, :]).astype(jnp.float32)
    return jnp.einsum("ijk,ck->cij", onehot, beam_taps.astype(jnp.float32)).astype(jnp.bfloat16)


def depthwise(cells, kernel):
    out = lax.conv_general_dilated(
        cells[None],
        kernel,
        window_strides=(1, 1),
        padding="VALID",
        dimension_numbers=("NCHW", "OIHW", "NCHW"),
        feature_group_count=cells.shape[0],
        preferred_element_type=jnp.float32,
    )
    return out[0].astype(jnp.bfloat16)


def halos(cells, axis, dim):
    length = cells.shape[dim]
    count = lax.axis_size(axis)
    ends = count - 1
    before = lax.ppermute(
        lax.slice_in_dim(cells, length - HALF, length, axis=dim), axis, [(i, (i + 1) % count) for i in range(ends)]
    )
    after = lax.ppermute(
        lax.slice_in_dim(cells, 0, HALF, axis=dim), axis, [((i + 1) % count, i) for i in range(ends)]
    )
    return before, after


def assemble(cells, before, after, kernel, dim):
    length = cells.shape[dim]
    if length < 4 * HALF:
        return depthwise(jnp.concatenate([before, cells, after], axis=dim), kernel)
    head = lax.slice_in_dim(cells, 0, 2 * HALF, axis=dim)
    tail = lax.slice_in_dim(cells, length - 2 * HALF, length, axis=dim)
    middle = depthwise(cells, kernel)
    first = depthwise(jnp.concatenate([before, head], axis=dim), kernel)
    last = depthwise(jnp.concatenate([tail, after], axis=dim), kernel)
    return jnp.concatenate([first, middle, last], axis=dim)


def split_pass(cells, kernel, axis, dim):
    before, after = halos(cells, axis, dim)
    return assemble(cells, before, after, kernel, dim)


def band_of_rows(cells, before, after, kernel, start, rows):
    pick = lambda part: lax.dynamic_slice_in_dim(part, start, rows, axis=1)
    return assemble(pick(cells), pick(before), pick(after), kernel, 2)


def inverse_root(matrix):
    frob_norm = jnp.sqrt(jnp.sum(matrix * matrix) + 1e-06)
    current = matrix / frob_norm
    unit_matrix = jnp.eye(matrix.shape[0], dtype=jnp.float32)
    inverse = unit_matrix
    for iteration in range(NS_STEPS):
        correction = 0.5 * (
            3.0 * unit_matrix - jnp.dot(inverse, current, precision=lax.Precision.HIGHEST)
        )
        current = jnp.dot(current, correction, precision=lax.Precision.HIGHEST)
        inverse = jnp.dot(correction, inverse, precision=lax.Precision.HIGHEST)
    return inverse / jnp.sqrt(frob_norm)


def pixel_moments(coarse, whitened):
    outputs = jnp.dot(coarse, whitened, preferred_element_type=jnp.float32)
    cubed = (outputs * outputs * outputs).astype(jnp.bfloat16)
    return lax.dot_general(
        cubed, whitened, (((1,), (1,)), ((), ())), preferred_element_type=jnp.float32
    )


def total_sum(partial, axes):
    count = 1
    for axis in axes:
        count *= lax.axis_size(axis)
    flat = partial.reshape(count, partial.size // count)
    pieces = lax.all_to_all(flat, axes, 0, 0, tiled=True)
    piece = jnp.sum(pieces, axis=0)
    spread = jnp.broadcast_to(piece[None], (count,) + piece.shape)
    gathered = lax.all_to_all(spread, axes, 0, 0, tiled=True)
    return gathered.reshape(partial.shape)


def gathered_sum(partial, axes):
    count = 1
    for axis in axes:
        count *= lax.axis_size(axis)
    spread = jnp.broadcast_to(partial[None], (count,) + partial.shape)
    gathered = lax.all_to_all(spread, axes, 0, 0, tiled=True)
    return jnp.sum(gathered, axis=0)


def shards(sky_maps, beam_sigma, whitening, unmix_init):
    beam_taps = lax.optimization_barrier(make_taps(beam_sigma))
    channels, height, breadth = sky_maps.shape
    rowwise = split_pass(sky_maps, beam_taps[:, None, :, None], "row", 1)
    column_kernel = beam_taps[:, None, None, :]
    parts = lax.axis_size("freq")
    devices = parts * lax.axis_size("row") * lax.axis_size("col")
    block = height * breadth // parts
    total_pixels = block * devices
    if parts == 2 and height % parts == 0:
        side = lax.axis_index("freq")
        half = height // parts
        before, after = halos(rowwise, "col", 2)
        outgoing = band_of_rows(rowwise, before, after, column_kernel, (1 - side) * half, half)
        outgoing = outgoing.reshape(channels, block)
        incoming = lax.ppermute(outgoing, "freq", [(0, 1), (1, 0)])
        outgoing, rowwise, before, after = lax.optimization_barrier((outgoing, rowwise, before, after))
        local = band_of_rows(rowwise, before, after, column_kernel, side * half, half)
        local = local.reshape(channels, block)
        plane_sums = jnp.sum(outgoing, axis=1, dtype=jnp.float32) + jnp.sum(local, axis=1, dtype=jnp.float32)
        placed = jnp.zeros((parts * channels,), jnp.float32)
        placed = lax.dynamic_update_slice_in_dim(placed, plane_sums, side * channels, axis=0)
        channel_sums = gathered_sum(placed, ("freq", "row", "col"))
        means = channel_sums / total_pixels
        shift = jnp.dot(whitening.astype(jnp.float32), means, precision=lax.Precision.HIGHEST)
        mine = lax.dynamic_slice_in_dim(whitening, side * channels, channels, axis=1)
        theirs = lax.dynamic_slice_in_dim(whitening, (1 - side) * channels, channels, axis=1)
        mixed = jnp.dot(mine, local, preferred_element_type=jnp.float32) + jnp.dot(
            theirs, incoming, preferred_element_type=jnp.float32
        )
    else:
        smoothed = split_pass(rowwise, column_kernel, "col", 2)
        flattened = smoothed.reshape(channels, height * breadth)
        spectra = lax.all_to_all(flattened, "freq", split_axis=1, concat_axis=0, tiled=True)
        channel_sums = gathered_sum(jnp.sum(spectra, axis=1, dtype=jnp.float32), ("freq", "row", "col"))
        means = channel_sums / total_pixels
        shift = jnp.dot(whitening.astype(jnp.float32), means, precision=lax.Precision.HIGHEST)
        mixed = jnp.dot(whitening, spectra, preferred_element_type=jnp.float32)
    whitened = (mixed - shift[:, None]).astype(jnp.bfloat16)
    unmixing = unmix_init
    for iteration in range(ITERS):
        moments = pixel_moments(unmixing.astype(jnp.bfloat16), whitened)
        moments = total_sum(moments, ("freq", "row", "col"))
        updated = moments / total_pixels - 3.0 * unmixing
        gram = jnp.dot(updated, updated.T, precision=lax.Precision.HIGHEST)
        unmixing = jnp.dot(inverse_root(gram), updated, precision=lax.Precision.HIGHEST)
    sources = jnp.dot(
        unmixing.astype(jnp.bfloat16), whitened, preferred_element_type=jnp.float32
    ).astype(jnp.bfloat16)
    return (unmixing, sources)


def solution(mesh):
    return jax.shard_map(
        shards,
        mesh=mesh,
        in_specs=(P("freq", "row", "col"), P("freq"), P(), P()),
        out_specs=(P(), P(None, ("freq", "row", "col"))),
        check_vma=False,
    )
```

```python
import jax
import jax.numpy as jnp
from jax import lax
from jax.sharding import PartitionSpec as P

HALF = 8
ITERS = 2
NS_STEPS = 5


def with_halo(cells, sides, width):
    for axis, dim in sides:
        count = lax.axis_size(axis)
        ends = count - 1
        head = lax.slice_in_dim(cells, 0, width, axis=dim)
        tail = lax.slice_in_dim(cells, cells.shape[dim] - width, cells.shape[dim], axis=dim)
        cells = jnp.concatenate(
            [
                lax.ppermute(tail, axis, [(i, (i + 1) % count) for i in range(ends)]),
                cells,
                lax.ppermute(head, axis, [((i + 1) % count, i) for i in range(ends)]),
            ],
            axis=dim,
        )
    return cells


def make_taps(beam_sigma):
    offsets = jnp.arange(2 * HALF + 1, dtype=jnp.float32) - HALF
    shaped = jnp.exp(
        -(offsets[None, :] * offsets[None, :]) / (2.0 * beam_sigma[:, None] * beam_sigma[:, None])
    )
    return (shaped / jnp.sum(shaped, axis=1, keepdims=True)).astype(jnp.bfloat16)


def make_band(beam_taps, length):
    spread = beam_taps.shape[1]
    offsets = jnp.arange(length + spread - 1)[None, :] - jnp.arange(length)[:, None]
    onehot = (offsets[:, :, None] == jnp.arange(spread)[None, None, :]).astype(jnp.float32)
    return jnp.einsum("ijk,ck->cij", onehot, beam_taps.astype(jnp.float32)).astype(jnp.bfloat16)


def depthwise(cells, kernel):
    out = lax.conv_general_dilated(
        cells[None],
        kernel,
        window_strides=(1, 1),
        padding="VALID",
        dimension_numbers=("NCHW", "OIHW", "NCHW"),
        feature_group_count=cells.shape[0],
        preferred_element_type=jnp.float32,
    )
    return out[0].astype(jnp.bfloat16)


def flat_permute(cells, axis, pairs, dim):
    if dim != 1:
        return lax.ppermute(cells, axis, pairs)
    flat = cells.reshape(cells.shape[0], cells.shape[1] * cells.shape[2])
    return lax.ppermute(flat, axis, pairs).reshape(cells.shape)


def halos(cells, axis, dim):
    length = cells.shape[dim]
    count = lax.axis_size(axis)
    ends = count - 1
    before = flat_permute(
        lax.slice_in_dim(cells, length - HALF, length, axis=dim), axis, [(i, (i + 1) % count) for i in range(ends)], dim
    )
    after = flat_permute(
        lax.slice_in_dim(cells, 0, HALF, axis=dim), axis, [((i + 1) % count, i) for i in range(ends)], dim
    )
    return before, after


def assemble(cells, before, after, kernel, dim):
    length = cells.shape[dim]
    if length < 4 * HALF:
        return depthwise(jnp.concatenate([before, cells, after], axis=dim), kernel)
    head = lax.slice_in_dim(cells, 0, 2 * HALF, axis=dim)
    tail = lax.slice_in_dim(cells, length - 2 * HALF, length, axis=dim)
    middle = depthwise(cells, kernel)
    first = depthwise(jnp.concatenate([before, head], axis=dim), kernel)
    last = depthwise(jnp.concatenate([tail, after], axis=dim), kernel)
    return jnp.concatenate([first, middle, last], axis=dim)


def split_pass(cells, kernel, axis, dim):
    before, after = halos(cells, axis, dim)
    return assemble(cells, before, after, kernel, dim)


def band_of_rows(cells, before, after, kernel, start, rows):
    pick = lambda part: lax.dynamic_slice_in_dim(part, start, rows, axis=1)
    return assemble(pick(cells), pick(before), pick(after), kernel, 2)


def inverse_root(matrix):
    frob_norm = jnp.sqrt(jnp.sum(matrix * matrix) + 1e-06)
    current = matrix / frob_norm
    unit_matrix = jnp.eye(matrix.shape[0], dtype=jnp.float32)
    inverse = unit_matrix
    for iteration in range(NS_STEPS):
        correction = 0.5 * (
            3.0 * unit_matrix - jnp.dot(inverse, current, precision=lax.Precision.HIGHEST)
        )
        current = jnp.dot(current, correction, precision=lax.Precision.HIGHEST)
        inverse = jnp.dot(correction, inverse, precision=lax.Precision.HIGHEST)
    return inverse / jnp.sqrt(frob_norm)


def pixel_moments(coarse, whitened):
    outputs = jnp.dot(coarse, whitened, preferred_element_type=jnp.float32)
    cubed = (outputs * outputs * outputs).astype(jnp.bfloat16)
    return lax.dot_general(
        cubed, whitened, (((1,), (1,)), ((), ())), preferred_element_type=jnp.float32
    )


def total_sum(partial, axes):
    count = 1
    for axis in axes:
        count *= lax.axis_size(axis)
    flat = partial.reshape(count, partial.size // count)
    pieces = lax.all_to_all(flat, axes, 0, 0, tiled=True)
    piece = jnp.sum(pieces, axis=0)
    spread = jnp.broadcast_to(piece[None], (count,) + piece.shape)
    gathered = lax.all_to_all(spread, axes, 0, 0, tiled=True)
    return gathered.reshape(partial.shape)


def gathered_sum(partial, axes):
    count = 1
    for axis in axes:
        count *= lax.axis_size(axis)
    spread = jnp.broadcast_to(partial[None], (count,) + partial.shape)
    gathered = lax.all_to_all(spread, axes, 0, 0, tiled=True)
    return jnp.sum(gathered, axis=0)


def shards(sky_maps, beam_sigma, whitening, unmix_init):
    beam_taps = lax.optimization_barrier(make_taps(beam_sigma))
    channels, height, breadth = sky_maps.shape
    rowwise = split_pass(sky_maps, beam_taps[:, None, :, None], "row", 1)
    column_kernel = beam_taps[:, None, None, :]
    parts = lax.axis_size("freq")
    devices = parts * lax.axis_size("row") * lax.axis_size("col")
    block = height * breadth // parts
    total_pixels = block * devices
    if parts == 2 and height % parts == 0:
        side = lax.axis_index("freq")
        half = height // parts
        width = channels // 2 if channels % 2 == 0 else channels
        spans = [(low, min(low + width, channels)) for low in range(0, channels, width)]
        theirs = lax.dynamic_slice_in_dim(whitening, (1 - side) * channels, channels, axis=1)
        sends, frames, partial = [], [], None
        for low, high in spans:
            rows = rowwise[low:high]
            before, after = halos(rows, "col", 2)
            outgoing = band_of_rows(rows, before, after, column_kernel[low:high], (1 - side) * half, half)
            outgoing = outgoing.reshape(high - low, block)
            incoming = lax.ppermute(outgoing, "freq", [(0, 1), (1, 0)])
            outgoing, rowwise, before, after = lax.optimization_barrier((outgoing, rowwise, before, after))
            sends.append(outgoing)
            frames.append((before, after))
            term = jnp.dot(theirs[:, low:high], incoming, preferred_element_type=jnp.float32)
            partial = term if partial is None else partial + term
        local = jnp.concatenate(
            [
                band_of_rows(rowwise[low:high], before, after, column_kernel[low:high], side * half, half)
                for (low, high), (before, after) in zip(spans, frames)
            ]
        ).reshape(channels, block)
        outgoing = jnp.concatenate(sends)
        plane_sums = jnp.sum(outgoing, axis=1, dtype=jnp.float32) + jnp.sum(local, axis=1, dtype=jnp.float32)
        placed = jnp.zeros((parts * channels,), jnp.float32)
        placed = lax.dynamic_update_slice_in_dim(placed, plane_sums, side * channels, axis=0)
        channel_sums = gathered_sum(placed, ("freq", "row", "col"))
        means = channel_sums / total_pixels
        shift = jnp.dot(whitening.astype(jnp.float32), means, precision=lax.Precision.HIGHEST)
        mine = lax.dynamic_slice_in_dim(whitening, side * channels, channels, axis=1)
        mixed = jnp.dot(mine, local, preferred_element_type=jnp.float32) + partial
    else:
        smoothed = split_pass(rowwise, column_kernel, "col", 2)
        flattened = smoothed.reshape(channels, height * breadth)
        spectra = lax.all_to_all(flattened, "freq", split_axis=1, concat_axis=0, tiled=True)
        channel_sums = gathered_sum(jnp.sum(spectra, axis=1, dtype=jnp.float32), ("freq", "row", "col"))
        means = channel_sums / total_pixels
        shift = jnp.dot(whitening.astype(jnp.float32), means, precision=lax.Precision.HIGHEST)
        mixed = jnp.dot(whitening, spectra, preferred_element_type=jnp.float32)
    whitened = (mixed - shift[:, None]).astype(jnp.bfloat16)
    unmixing = unmix_init
    for iteration in range(ITERS):
        moments = pixel_moments(unmixing.astype(jnp.bfloat16), whitened)
        moments = total_sum(moments, ("freq", "row", "col"))
        updated = moments / total_pixels - 3.0 * unmixing
        gram = jnp.dot(updated, updated.T, precision=lax.Precision.HIGHEST)
        unmixing = jnp.dot(inverse_root(gram), updated, precision=lax.Precision.HIGHEST)
    sources = jnp.dot(
        unmixing.astype(jnp.bfloat16), whitened, preferred_element_type=jnp.float32
    ).astype(jnp.bfloat16)
    return (unmixing, sources)


def solution(mesh):
    return jax.shard_map(
        shards,
        mesh=mesh,
        in_specs=(P("freq", "row", "col"), P("freq"), P(), P()),
        out_specs=(P(), P(None, ("freq", "row", "col"))),
        check_vma=False,
    )
```

```python
import jax
import jax.numpy as jnp
from jax import lax
from jax.sharding import PartitionSpec as P

HALF = 8
ITERS = 2
NS_STEPS = 5


def with_halo(cells, sides, width):
    for axis, dim in sides:
        count = lax.axis_size(axis)
        ends = count - 1
        head = lax.slice_in_dim(cells, 0, width, axis=dim)
        tail = lax.slice_in_dim(cells, cells.shape[dim] - width, cells.shape[dim], axis=dim)
        cells = jnp.concatenate(
            [
                lax.ppermute(tail, axis, [(i, (i + 1) % count) for i in range(ends)]),
                cells,
                lax.ppermute(head, axis, [((i + 1) % count, i) for i in range(ends)]),
            ],
            axis=dim,
        )
    return cells


def make_taps(beam_sigma):
    offsets = jnp.arange(2 * HALF + 1, dtype=jnp.float32) - HALF
    shaped = jnp.exp(
        -(offsets[None, :] * offsets[None, :]) / (2.0 * beam_sigma[:, None] * beam_sigma[:, None])
    )
    return (shaped / jnp.sum(shaped, axis=1, keepdims=True)).astype(jnp.bfloat16)


def make_band(beam_taps, length):
    spread = beam_taps.shape[1]
    offsets = jnp.arange(length + spread - 1)[None, :] - jnp.arange(length)[:, None]
    onehot = (offsets[:, :, None] == jnp.arange(spread)[None, None, :]).astype(jnp.float32)
    return jnp.einsum("ijk,ck->cij", onehot, beam_taps.astype(jnp.float32)).astype(jnp.bfloat16)


def depthwise(cells, kernel):
    out = lax.conv_general_dilated(
        cells[None],
        kernel,
        window_strides=(1, 1),
        padding="VALID",
        dimension_numbers=("NCHW", "OIHW", "NCHW"),
        feature_group_count=cells.shape[0],
        preferred_element_type=jnp.float32,
    )
    return out[0].astype(jnp.bfloat16)


def flat_permute(cells, axis, pairs, dim):
    if dim != 1:
        return lax.ppermute(cells, axis, pairs)
    flat = cells.reshape(cells.shape[0], cells.shape[1] * cells.shape[2])
    return lax.ppermute(flat, axis, pairs).reshape(cells.shape)


def halos(cells, axis, dim):
    length = cells.shape[dim]
    count = lax.axis_size(axis)
    ends = count - 1
    before = flat_permute(
        lax.slice_in_dim(cells, length - HALF, length, axis=dim), axis, [(i, (i + 1) % count) for i in range(ends)], dim
    )
    after = flat_permute(
        lax.slice_in_dim(cells, 0, HALF, axis=dim), axis, [((i + 1) % count, i) for i in range(ends)], dim
    )
    return before, after


def assemble(cells, before, after, kernel, dim):
    length = cells.shape[dim]
    if length < 4 * HALF:
        return depthwise(jnp.concatenate([before, cells, after], axis=dim), kernel)
    head = lax.slice_in_dim(cells, 0, 2 * HALF, axis=dim)
    tail = lax.slice_in_dim(cells, length - 2 * HALF, length, axis=dim)
    middle = depthwise(cells, kernel)
    first = depthwise(jnp.concatenate([before, head], axis=dim), kernel)
    last = depthwise(jnp.concatenate([tail, after], axis=dim), kernel)
    return jnp.concatenate([first, middle, last], axis=dim)


def split_pass(cells, kernel, axis, dim):
    before, after = halos(cells, axis, dim)
    return assemble(cells, before, after, kernel, dim)


def band_of_rows(cells, before, after, kernel, start, rows):
    pick = lambda part: lax.dynamic_slice_in_dim(part, start, rows, axis=1)
    return assemble(pick(cells), pick(before), pick(after), kernel, 2)


def inverse_root(matrix):
    frob_norm = jnp.sqrt(jnp.sum(matrix * matrix) + 1e-06)
    current = matrix / frob_norm
    unit_matrix = jnp.eye(matrix.shape[0], dtype=jnp.float32)
    inverse = unit_matrix
    for iteration in range(NS_STEPS):
        correction = 0.5 * (
            3.0 * unit_matrix - jnp.dot(inverse, current, precision=lax.Precision.HIGHEST)
        )
        current = jnp.dot(current, correction, precision=lax.Precision.HIGHEST)
        inverse = jnp.dot(correction, inverse, precision=lax.Precision.HIGHEST)
    return inverse / jnp.sqrt(frob_norm)


def pixel_moments(coarse, whitened):
    outputs = jnp.dot(coarse, whitened, preferred_element_type=jnp.float32)
    cubed = (outputs * outputs * outputs).astype(jnp.bfloat16)
    return lax.dot_general(
        cubed, whitened, (((1,), (1,)), ((), ())), preferred_element_type=jnp.float32
    )


def total_sum(partial, axes):
    count = 1
    for axis in axes:
        count *= lax.axis_size(axis)
    flat = partial.reshape(count, partial.size // count)
    pieces = lax.all_to_all(flat, axes, 0, 0, tiled=True)
    piece = jnp.sum(pieces, axis=0)
    spread = jnp.broadcast_to(piece[None], (count,) + piece.shape)
    gathered = lax.all_to_all(spread, axes, 0, 0, tiled=True)
    return gathered.reshape(partial.shape)


def gathered_sum(partial, axes):
    count = 1
    for axis in axes:
        count *= lax.axis_size(axis)
    spread = jnp.broadcast_to(partial[None], (count,) + partial.shape)
    gathered = lax.all_to_all(spread, axes, 0, 0, tiled=True)
    return jnp.sum(gathered, axis=0)


def shards(sky_maps, beam_sigma, whitening, unmix_init):
    beam_taps = lax.optimization_barrier(make_taps(beam_sigma))
    channels, height, breadth = sky_maps.shape
    rowwise = split_pass(sky_maps, beam_taps[:, None, :, None], "row", 1)
    column_kernel = beam_taps[:, None, None, :]
    parts = lax.axis_size("freq")
    devices = parts * lax.axis_size("row") * lax.axis_size("col")
    block = height * breadth // parts
    total_pixels = block * devices
    if parts == 2 and height % parts == 0:
        side = lax.axis_index("freq")
        half = height // parts
        width = channels // 2 if channels % 2 == 0 else channels
        spans = [(low, min(low + width, channels)) for low in range(0, channels, width)]
        theirs = lax.dynamic_slice_in_dim(whitening, (1 - side) * channels, channels, axis=1)
        sends, frames, partial = [], [], None
        for low, high in spans:
            rows = rowwise[low:high]
            before, after = halos(rows, "col", 2)
            outgoing = band_of_rows(rows, before, after, column_kernel[low:high], (1 - side) * half, half)
            outgoing = outgoing.reshape(high - low, block)
            incoming = lax.ppermute(outgoing, "freq", [(0, 1), (1, 0)])
            outgoing, rowwise, before, after = lax.optimization_barrier((outgoing, rowwise, before, after))
            sends.append(outgoing)
            frames.append((before, after))
            term = jnp.dot(theirs[:, low:high], incoming, preferred_element_type=jnp.float32)
            partial = term if partial is None else partial + term
        local = jnp.concatenate(
            [
                band_of_rows(rowwise[low:high], before, after, column_kernel[low:high], side * half, half)
                for (low, high), (before, after) in zip(spans, frames)
            ]
        ).reshape(channels, block)
        outgoing = jnp.concatenate(sends)
        plane_sums = jnp.sum(outgoing, axis=1, dtype=jnp.float32) + jnp.sum(local, axis=1, dtype=jnp.float32)
        count = devices
        spread = jnp.broadcast_to(plane_sums[None], (count, channels))
        gathered = lax.all_to_all(spread, ("freq", "row", "col"), 0, 0, tiled=True)
        channel_sums = jnp.sum(gathered.reshape(parts, count // parts, channels), axis=1).reshape(parts * channels)
        means = channel_sums / total_pixels
        shift = jnp.dot(whitening.astype(jnp.float32), means, precision=lax.Precision.HIGHEST)
        mine = lax.dynamic_slice_in_dim(whitening, side * channels, channels, axis=1)
        mixed = jnp.dot(mine, local, preferred_element_type=jnp.float32) + partial
    else:
        smoothed = split_pass(rowwise, column_kernel, "col", 2)
        flattened = smoothed.reshape(channels, height * breadth)
        spectra = lax.all_to_all(flattened, "freq", split_axis=1, concat_axis=0, tiled=True)
        channel_sums = gathered_sum(jnp.sum(spectra, axis=1, dtype=jnp.float32), ("freq", "row", "col"))
        means = channel_sums / total_pixels
        shift = jnp.dot(whitening.astype(jnp.float32), means, precision=lax.Precision.HIGHEST)
        mixed = jnp.dot(whitening, spectra, preferred_element_type=jnp.float32)
    whitened = (mixed - shift[:, None]).astype(jnp.bfloat16)
    unmixing = unmix_init
    for iteration in range(ITERS):
        moments = pixel_moments(unmixing.astype(jnp.bfloat16), whitened)
        moments = total_sum(moments, ("freq", "row", "col"))
        updated = moments / total_pixels - 3.0 * unmixing
        gram = jnp.dot(updated, updated.T, precision=lax.Precision.HIGHEST)
        unmixing = jnp.dot(inverse_root(gram), updated, precision=lax.Precision.HIGHEST)
    sources = jnp.dot(
        unmixing.astype(jnp.bfloat16), whitened, preferred_element_type=jnp.float32
    ).astype(jnp.bfloat16)
    return (unmixing, sources)


def solution(mesh):
    return jax.shard_map(
        shards,
        mesh=mesh,
        in_specs=(P("freq", "row", "col"), P("freq"), P(), P()),
        out_specs=(P(), P(None, ("freq", "row", "col"))),
        check_vma=False,
    )
```
